512 devices in a mesh: pts: 128 (over z, x, core), grp: 4 (over y).
Axes of the slice: x: 4, y: 4, z: 16, core: 2. Of those that a mesh axis runs over, the one named last changes fastest.
Arguments:
- jac_cam: float32 [12, 4, 524288], P(None, None, ('pts', 'grp')), may hold values from -2 to 2
- jac_pt: float32 [6, 4, 524288], P(None, None, ('pts', 'grp')), may hold values from -7 to 7
- resid: float32 [2, 4, 524288], P(None, None, ('pts', 'grp')), may hold values from -6 to 6
- obs_slot: int32 [4, 524288], P(None, ('pts', 'grp')), may hold values from 0 to 2047, as said below
- requests: int32 [4, 4, 4, 16384], P('grp', None, None, 'pts'), may hold values from -1 to 255, as said below
- coloring: int32 [131072], P(('pts', 'grp')), may hold values 0 or 1
- damping: float32 [1], replicated, may hold values from 0.5 to 4
Outputs:
- cam_step: float32 [6, 131072], P(None, ('pts', 'grp'))
- point_step: float32 [3, 524288], P(None, ('pts', 'grp'))
The draws below stay inside these ranges and needn't reach their ends.
Inputs may be any that keep to these rules, and one draw needn't show every extreme that they name: `requests`: in each row of a device toward one owner the live entries come first and name distinct cameras; any device may fill all 4 slots toward any owner device, and every device fills all 4 slots toward one owner device common to all devices. `obs_slot`: every entry names a live slot of its device's request table; the 4 observations of a point name distinct slots.
All inputs are finite; a program needn't handle non-finite values. No bound on the sum of `coloring` on one device may be relied on, other than what follows from the above.
Results may differ from the reference program's by a relative error of at most 0.0003.
Values sent between devices are 32-bit elements; how exact they have to be, the bound alone decides.
No kernel may reach another device: no remote copies, remote signals or barrier semaphores. Data moves between devices by JAX's collectives and lax.ppermute only.
A program may use at most 64 MiB of HBM per device.

```python
import math
import jax
import jax.numpy as jnp
from jax import lax

PT_DEV = 1024
CAM_DEV = 256
OBS = 4
CAP = 4
ROUNDS = 2
NPTS = 524288
NCAM = 131072
N_PTS = 128
N_GRP = 4


def slot_layout(key):
    devices = N_PTS * N_GRP
    key_list = jax.random.split(jax.random.fold_in(key, 7), 5)
    counts = jax.random.randint(key_list[0], (devices, devices), CAP // 2 + 1, CAP + 1)
    hottest = jax.random.randint(key_list[2], (), 0, devices)
    column = jnp.arange(devices)[None, :]
    filled = (column == hottest) | (column == 0) | (column == devices - 1)
    counts = jnp.where(filled, CAP, counts)
    offsets = jax.random.randint(key_list[3], (devices, devices), 0, CAM_DEV)
    return (counts, offsets, key_list[4])


def draw_requests(key, part):
    counts, offsets, spare = slot_layout(key)
    places = jnp.arange(CAP, dtype=jnp.int32)[None, None, :]
    cameras = (offsets[:, :, None] + places) % CAM_DEV
    table = jnp.where(places < counts[:, :, None], cameras, -1)
    table = table.reshape(N_PTS, N_GRP, N_PTS, N_GRP, CAP).transpose(1, 3, 4, 0, 2)
    return table.reshape(N_GRP, N_GRP, CAP, N_PTS * N_PTS).astype(jnp.int32)


def draw_obs_slot(key, part):
    counts, offsets, spare = slot_layout(key)
    devices = N_PTS * N_GRP
    width = N_GRP * CAP * N_PTS
    owner = jnp.arange(N_PTS)[None, None, :] * N_GRP + jnp.arange(N_GRP)[:, None, None]
    places = jnp.arange(CAP)[None, None, :, None]
    live = (places < counts[:, owner]).reshape(devices, width)
    index = jnp.arange(width, dtype=jnp.int32)[None, :]
    score = jnp.where(live, index, index + width)
    order = jnp.argsort(score, axis=1, stable=True).astype(jnp.int32)
    alive = jnp.sum(live.astype(jnp.int32), axis=1)
    point_index = jnp.arange(NPTS, dtype=jnp.int32)
    point_device = point_index // PT_DEV
    point_local = point_index % PT_DEV
    limit = alive[point_device]
    jitter = jax.random.randint(spare, (NPTS,), 0, OBS)
    start = (point_local * OBS + jitter) % limit
    start = jnp.where(point_local == 0, limit - 1, start)
    rank = (start[None, :] + jnp.arange(OBS, dtype=jnp.int32)[:, None]) % limit[None, :]
    return order[point_device[None, :], rank].astype(jnp.int32)


def common_part(key, shape, scale, lowest, highest):
    signs = jnp.where(jax.random.bernoulli(key, 0.5, shape), 1.0, -1.0)
    magnitude = jax.random.uniform(jax.random.fold_in(key, 1), shape, minval=lowest, maxval=highest)
    return scale * signs * magnitude


def rough_factor(key, shape):
    return jnp.exp(jax.random.uniform(key, shape, minval=-0.5, maxval=0.5))


def draw_jac_cam(key, part):
    common_key, noise_key, factor_key = jax.random.split(jax.random.fold_in(key, 11), 3)
    shape = (12, OBS, NPTS)
    common = common_part(common_key, (12, 1, 1), 0.25, 0.7, 1.3)
    noise = 0.25 * jnp.clip(jax.random.normal(noise_key, shape), -3.0, 3.0)
    factor = rough_factor(factor_key, (1, OBS, NPTS))
    return (factor * (common + noise)).astype(jnp.float32)


def draw_jac_pt(key, part):
    common_key, noise_key, factor_key = jax.random.split(jax.random.fold_in(key, 13), 3)
    shape = (6, OBS, NPTS)
    common = common_part(common_key, (6, 1, 1), 2.0, 0.7, 1.3)
    noise = 0.5 * jnp.clip(jax.random.normal(noise_key, shape), -3.0, 3.0)
    factor = rough_factor(factor_key, (1, OBS, NPTS))
    return (factor * (common + noise)).astype(jnp.float32)


def draw_resid(key, part):
    common_key, noise_key = jax.random.split(jax.random.fold_in(key, 17), 2)
    shape = (2, OBS, NPTS)
    common = common_part(common_key, (2, 1, 1), 1.0, 1.0, 2.0)
    noise = jnp.clip(jax.random.normal(noise_key, shape), -4.0, 4.0)
    return (common + noise).astype(jnp.float32)


def set_ends(values, own_key, smallest, largest):
    shape = values.shape
    index_at = [jax.random.randint(jax.random.fold_in(own_key, axis), (), 0, shape[axis]) for axis in range(len(shape))]
    values = values.at[tuple(index_at)].set(smallest)
    longest = shape.index(max(shape))
    index_at[longest] = (index_at[longest] + 1) % shape[longest]
    return values.at[tuple(index_at)].set(largest)


def setup_inputs(seed: int = 0) -> dict:
    splits = jax.random.split(jax.random.key(seed), 8)
    return {
        "jac_cam": draw_jac_cam(jax.random.fold_in(splits[7], 71), 0),
        "jac_pt": draw_jac_pt(jax.random.fold_in(splits[7], 71), 0),
        "resid": draw_resid(jax.random.fold_in(splits[7], 71), 0),
        "obs_slot": draw_obs_slot(jax.random.fold_in(splits[7], 71), 0),
        "requests": draw_requests(jax.random.fold_in(splits[7], 71), 0),
        "coloring": set_ends((jax.random.randint(splits[5], (NCAM,), 0, 2) < 1).astype(jnp.int32), jax.random.fold_in(splits[5], 1), 0, 1),
        "damping": jnp.clip(jnp.exp(jax.random.uniform(splits[6], (1,), jnp.float32, math.log(0.5), math.log(4.0))), 0.5, 4.0),
    }


UPPER = [(first, second) for first in range(6) for second in range(first, 6)]

def pack_sym(matrix):
    return jnp.stack([matrix[first, second] for first, second in UPPER])

def unpack_sym(packed):
    rows = []
    for first in range(6):
        rows.append(jnp.stack([packed[UPPER.index((min(first, second), max(first, second)))] for second in range(6)]))
    return jnp.stack(rows)

def invert_three(matrix):
    c00 = matrix[1, 1] * matrix[2, 2] - matrix[1, 2] * matrix[2, 1]
    c01 = matrix[1, 2] * matrix[2, 0] - matrix[1, 0] * matrix[2, 2]
    c02 = matrix[1, 0] * matrix[2, 1] - matrix[1, 1] * matrix[2, 0]
    c11 = matrix[0, 0] * matrix[2, 2] - matrix[0, 2] * matrix[2, 0]
    c12 = matrix[0, 2] * matrix[1, 0] - matrix[0, 0] * matrix[1, 2]
    c22 = matrix[0, 0] * matrix[1, 1] - matrix[0, 1] * matrix[1, 0]
    determinant = matrix[0, 0] * c00 + matrix[0, 1] * c01 + matrix[0, 2] * c02
    rows = [[c00, c01, c02], [c01, c11, c12], [c02, c12, c22]]
    return jnp.stack([jnp.stack([entry / determinant for entry in line]) for line in rows])

def cholesky_six(matrix):
    lower = {}
    for first in range(6):
        for second in range(first + 1):
            total = matrix[first, second]
            for inner in range(second):
                total = total - lower[first, inner] * lower[second, inner]
            if first == second:
                lower[first, first] = jnp.sqrt(total)
            else:
                lower[first, second] = total / lower[second, second]
    return lower

def solve_six(lower, target):
    middle = []
    for first in range(6):
        total = target[first]
        for inner in range(first):
            total = total - lower[first, inner] * middle[inner]
        middle.append(total / lower[first, first])
    result = [None] * 6
    for first in reversed(range(6)):
        total = middle[first]
        for inner in range(first + 1, 6):
            total = total - lower[inner, first] * result[inner]
        result[first] = total / lower[first, first]
    return jnp.stack(result)

def point_geometry(jac_cam, jac_pt, resid, damp_value):
    camera_part = jac_cam.reshape((2, 6) + jac_cam.shape[1:])
    point_part = jac_pt.reshape((2, 3) + jac_pt.shape[1:])
    coupling = lax.optimization_barrier(jnp.sum(camera_part[:, :, None] * point_part[:, None, :], axis=0))
    normal = lax.optimization_barrier(jnp.sum(point_part[:, :, None] * point_part[:, None, :], axis=(0, 3)))
    normal = normal + damp_value * jnp.eye(3, dtype=jac_pt.dtype)[:, :, None]
    point_inverse = invert_three(normal)
    point_rhs = -lax.optimization_barrier(jnp.sum(point_part * resid[:, None], axis=(0, 2)))
    return (camera_part, coupling, point_inverse, point_rhs)

def camera_terms(camera_part, coupling, point_inverse, point_rhs, resid):
    weighted = lax.optimization_barrier(jnp.sum(coupling[:, :, None] * point_inverse[None, :, :, None, :], axis=1))
    schur_part = lax.optimization_barrier(jnp.sum(weighted[:, None] * coupling[None], axis=2))
    camera_block = lax.optimization_barrier(jnp.sum(camera_part[:, :, None] * camera_part[:, None, :], axis=0))
    camera_rhs = -lax.optimization_barrier(jnp.sum(camera_part * resid[:, None], axis=0)) - lax.optimization_barrier(jnp.sum(weighted * point_rhs[None, :, None, :], axis=1))
    return jnp.concatenate([pack_sym(camera_block), pack_sym(schur_part), camera_rhs], axis=0)

def point_side(coupling, obs_steps):
    return lax.optimization_barrier(jnp.sum(coupling * obs_steps[:, None], axis=(0, 2)))

def camera_side(coupling, point_inverse, point_sum):
    solved = lax.optimization_barrier(jnp.sum(point_inverse * point_sum[None], axis=1))
    return lax.optimization_barrier(jnp.sum(coupling * solved[None, :, None, :], axis=1))

def owner_setup(totals, damp_value):
    upper_block = unpack_sym(totals[:21]) + damp_value * jnp.eye(6, dtype=totals.dtype)[:, :, None]
    diagonal_block = upper_block - unpack_sym(totals[21:42])
    return (upper_block, cholesky_six(diagonal_block), totals[42:48])

def reference(jac_cam, jac_pt, resid, obs_slot, requests, coloring, damping):
    damp_value = damping[0]
    devices = N_PTS * N_GRP
    cam_total = CAM_DEV * devices

    def blocks(array):
        return array.reshape(array.shape[0], OBS, devices, PT_DEV).transpose(2, 0, 1, 3)
    items = (jnp.arange(devices, dtype=jnp.int32), blocks(jac_cam), blocks(jac_pt), blocks(resid), obs_slot.reshape(OBS, devices, PT_DEV).transpose(1, 0, 2))

    def camera_ids(device, slots):
        row_pts = device // N_GRP
        row_grp = device % N_GRP
        owner_grp = slots // (CAP * N_PTS)
        place = slots // N_PTS % CAP
        owner_pts = slots % N_PTS
        local = requests[row_grp, owner_grp, place, row_pts * N_PTS + owner_pts]
        return ((owner_pts * N_GRP + owner_grp) * CAM_DEV + local).astype(jnp.int32)

    def build(carry, item):
        device, camera_block, point_block, res_block, slots = item
        camera_part, coupling, point_inverse, point_rhs = point_geometry(camera_block, point_block, res_block, damp_value)
        terms = camera_terms(camera_part, coupling, point_inverse, point_rhs, res_block)
        ids = camera_ids(device, slots).reshape(-1)
        added = jax.ops.segment_sum(terms.reshape(terms.shape[0], -1).T, ids, num_segments=cam_total).T
        return (carry + added, None)
    totals, unused = lax.scan(build, jnp.zeros((48, cam_total), jac_cam.dtype), items)
    upper_block, factor, camera_rhs = owner_setup(totals, damp_value)

    def apply_schur(steps):

        def visit(carry, item):
            device, camera_block, point_block, res_block, slots = item
            camera_part, coupling, point_inverse, point_rhs = point_geometry(camera_block, point_block, res_block, damp_value)
            ids = camera_ids(device, slots)
            point_sum = point_side(coupling, jnp.take(steps, ids, axis=1))
            pushed = camera_side(coupling, point_inverse, point_sum)
            added = jax.ops.segment_sum(pushed.reshape(6, -1).T, ids.reshape(-1), num_segments=cam_total).T
            return (carry + added, None)
        pushed_total, unused_rows = lax.scan(visit, jnp.zeros((6, cam_total), jac_cam.dtype), items)
        return lax.optimization_barrier(jnp.sum(upper_block * steps[None], axis=1)) - pushed_total
    colors = [coloring == 0, coloring == 1]
    steps = jnp.where(colors[0][None], solve_six(factor, camera_rhs), 0.0)
    for sweep in range(2 * ROUNDS - 1):
        current = colors[(sweep + 1) % 2]
        product = apply_schur(steps)
        steps = steps + jnp.where(current[None], solve_six(factor, camera_rhs - product), 0.0)

    def finish(carry, item):
        device, camera_block, point_block, res_block, slots = item
        camera_part, coupling, point_inverse, point_rhs = point_geometry(camera_block, point_block, res_block, damp_value)
        point_sum = point_side(coupling, jnp.take(steps, camera_ids(device, slots), axis=1))
        return (carry, lax.optimization_barrier(jnp.sum(point_inverse * (point_rhs - point_sum)[None], axis=1)))
    unused_carry, point_rows = lax.scan(finish, jnp.zeros((), jac_cam.dtype), items)
    point_step = point_rows.transpose(1, 0, 2).reshape(3, devices * PT_DEV)
    return (steps, point_step)
```

```python
import jax
import jax.numpy as jnp
from jax import lax
from jax.sharding import Mesh, PartitionSpec as P

ROUNDS = 2


UPPER = [(first, second) for first in range(6) for second in range(first, 6)]


def pack_sym(matrix):
    return jnp.stack([matrix[first, second] for first, second in UPPER])


def unpack_sym(packed):
    rows = []
    for first in range(6):
        rows.append(
            jnp.stack(
                [
                    packed[UPPER.index((min(first, second), max(first, second)))]
                    for second in range(6)
                ]
            )
        )
    return jnp.stack(rows)


def invert_three(matrix):
    c00 = matrix[1, 1] * matrix[2, 2] - matrix[1, 2] * matrix[2, 1]
    c01 = matrix[1, 2] * matrix[2, 0] - matrix[1, 0] * matrix[2, 2]
    c02 = matrix[1, 0] * matrix[2, 1] - matrix[1, 1] * matrix[2, 0]
    c11 = matrix[0, 0] * matrix[2, 2] - matrix[0, 2] * matrix[2, 0]
    c12 = matrix[0, 2] * matrix[1, 0] - matrix[0, 0] * matrix[1, 2]
    c22 = matrix[0, 0] * matrix[1, 1] - matrix[0, 1] * matrix[1, 0]
    determinant = matrix[0, 0] * c00 + matrix[0, 1] * c01 + matrix[0, 2] * c02
    rows = [[c00, c01, c02], [c01, c11, c12], [c02, c12, c22]]
    return jnp.stack([jnp.stack([entry / determinant for entry in line]) for line in rows])


def cholesky_six(matrix):
    lower = {}
    for first in range(6):
        for second in range(first + 1):
            total = matrix[first, second]
            for inner in range(second):
                total = total - lower[first, inner] * lower[second, inner]
            if first == second:
                lower[first, first] = jnp.sqrt(total)
            else:
                lower[first, second] = total / lower[second, second]
    return lower


def solve_six(lower, target):
    middle = []
    for first in range(6):
        total = target[first]
        for inner in range(first):
            total = total - lower[first, inner] * middle[inner]
        middle.append(total / lower[first, first])
    result = [None] * 6
    for first in reversed(range(6)):
        total = middle[first]
        for inner in range(first + 1, 6):
            total = total - lower[inner, first] * result[inner]
        result[first] = total / lower[first, first]
    return jnp.stack(result)


def point_geometry(jac_cam, jac_pt, resid, damp_value):
    camera_part = jac_cam.reshape((2, 6) + jac_cam.shape[1:])
    point_part = jac_pt.reshape((2, 3) + jac_pt.shape[1:])
    coupling = jnp.sum(camera_part[:, :, None] * point_part[:, None, :], axis=0)
    normal = jnp.sum(point_part[:, :, None] * point_part[:, None, :], axis=(0, 3))
    normal = normal + damp_value * jnp.eye(3, dtype=jac_pt.dtype)[:, :, None]
    point_inverse = invert_three(normal)
    point_rhs = -jnp.sum(point_part * resid[:, None], axis=(0, 2))
    return (camera_part, coupling, point_inverse, point_rhs)


def camera_terms(camera_part, coupling, point_inverse, point_rhs, resid):
    weighted = jnp.sum(coupling[:, :, None] * point_inverse[None, :, :, None, :], axis=1)
    schur_part = jnp.sum(weighted[:, None] * coupling[None], axis=2)
    camera_block = jnp.sum(camera_part[:, :, None] * camera_part[:, None, :], axis=0)
    camera_rhs = -jnp.sum(camera_part * resid[:, None], axis=0) - jnp.sum(
        weighted * point_rhs[None, :, None, :], axis=1
    )
    return jnp.concatenate([pack_sym(camera_block), pack_sym(schur_part), camera_rhs], axis=0)


def point_side(coupling, obs_steps):
    return jnp.sum(coupling * obs_steps[:, None], axis=(0, 2))


def camera_side(coupling, point_inverse, point_sum):
    solved = jnp.sum(point_inverse * point_sum[None], axis=1)
    return jnp.sum(coupling * solved[None, :, None, :], axis=1)


def owner_setup(totals, damp_value):
    upper_block = unpack_sym(totals[:21]) + damp_value * jnp.eye(6, dtype=totals.dtype)[:, :, None]
    diagonal_block = upper_block - unpack_sym(totals[21:42])
    return (upper_block, cholesky_six(diagonal_block), totals[42:48])


def owner_sum(received, owner_index, segments):
    features = received.shape[0]
    summed = jax.ops.segment_sum(
        received.reshape(features, -1).T, owner_index.reshape(-1), num_segments=segments + 1
    )
    return summed[:segments].T


def exchange(values):
    features, groups, places, lanes = values.shape
    inner = lanes // OUTER
    t = values.reshape(features, groups, places, OUTER, inner).transpose(4, 1, 3, 2, 0)
    t = t.reshape(inner * groups, OUTER, places, features)
    t = lax.all_to_all(t, INNER_AXES, 0, 0, tiled=True)
    t = lax.all_to_all(t, "z", 1, 1, tiled=True)
    t = t.reshape(inner, groups, OUTER, places, features).transpose(4, 1, 3, 2, 0)
    return t.reshape(features, groups, places, lanes)


def shards(jac_cam, jac_pt, resid, obs_slot, requests, coloring, damping):
    damp_value = damping[0]
    table = requests[0]
    cam_count = coloring.shape[0]
    slot_count = table.size
    flat_slots = obs_slot.reshape(-1)
    camera_part, coupling, point_inverse, point_rhs = point_geometry(
        jac_cam, jac_pt, resid, damp_value
    )
    terms = camera_terms(camera_part, coupling, point_inverse, point_rhs, resid)

    def slot_totals(values):
        features = values.shape[0]
        summed = jax.ops.segment_sum(
            values.reshape(features, -1).T, flat_slots, num_segments=slot_count
        ).T
        return summed.reshape((features,) + table.shape)

    def at_observations(slot_values):
        return jnp.take(slot_values.reshape(slot_values.shape[0], -1), obs_slot, axis=1)

    sent = jnp.concatenate([slot_totals(terms), table[None].astype(terms.dtype)], axis=0)
    arrived_all = exchange(sent)
    blocks_back = arrived_all[:-1]
    served = arrived_all[-1].astype(jnp.int32)
    valid = served >= 0
    owner_index = jnp.where(valid, served, cam_count)
    totals = owner_sum(blocks_back, owner_index, cam_count)

    def share_steps(step_values):
        reply = jnp.where(
            valid[None], jnp.take(step_values, jnp.where(valid, served, 0), axis=1), 0.0
        )
        arrived = exchange(reply)
        return at_observations(arrived)

    upper_block, factor, camera_rhs = owner_setup(totals, damp_value)
    colors = [coloring == 0, coloring == 1]
    steps = jnp.where(colors[0][None], solve_six(factor, camera_rhs), 0.0)
    for sweep in range(2 * ROUNDS - 1):
        current = colors[(sweep + 1) % 2]
        point_sum = point_side(coupling, share_steps(steps))
        pushed = camera_side(coupling, point_inverse, point_sum)
        back = exchange(slot_totals(pushed))
        product = jnp.sum(upper_block * steps[None], axis=1) - owner_sum(
            back, owner_index, cam_count
        )
        steps = steps + jnp.where(current[None], solve_six(factor, camera_rhs - product), 0.0)
    point_sum = point_side(coupling, share_steps(steps))
    point_step = jnp.sum(point_inverse * (point_rhs - point_sum)[None], axis=1)
    return (steps, point_step)


OUTER = 16
INNER_AXES = ("x", "c", "y")


def solution(mesh):
    npts, ngrp = mesh.shape["pts"], mesh.shape["grp"]
    split = Mesh(mesh.devices.reshape(OUTER, npts // OUTER, 1, ngrp), ("z", "x", "c", "y"))
    every = ("z", "x", "c", "y")
    return jax.shard_map(
        shards,
        mesh=split,
        in_specs=(
            P(None, None, every),
            P(None, None, every),
            P(None, None, every),
            P(None, every),
            P("y", None, None, ("z", "x", "c")),
            P(every),
            P(),
        ),
        out_specs=(P(None, every), P(None, every)),
        check_vma=False,
    )
```

```python
import jax
import jax.numpy as jnp
from jax import lax
from jax.sharding import Mesh, PartitionSpec as P

ROUNDS = 2


UPPER = [(first, second) for first in range(6) for second in range(first, 6)]


def pack_sym(matrix):
    return jnp.stack([matrix[first, second] for first, second in UPPER])


def unpack_sym(packed):
    rows = []
    for first in range(6):
        rows.append(
            jnp.stack(
                [
                    packed[UPPER.index((min(first, second), max(first, second)))]
                    for second in range(6)
                ]
            )
        )
    return jnp.stack(rows)


def invert_three(matrix):
    c00 = matrix[1, 1] * matrix[2, 2] - matrix[1, 2] * matrix[2, 1]
    c01 = matrix[1, 2] * matrix[2, 0] - matrix[1, 0] * matrix[2, 2]
    c02 = matrix[1, 0] * matrix[2, 1] - matrix[1, 1] * matrix[2, 0]
    c11 = matrix[0, 0] * matrix[2, 2] - matrix[0, 2] * matrix[2, 0]
    c12 = matrix[0, 2] * matrix[1, 0] - matrix[0, 0] * matrix[1, 2]
    c22 = matrix[0, 0] * matrix[1, 1] - matrix[0, 1] * matrix[1, 0]
    determinant = matrix[0, 0] * c00 + matrix[0, 1] * c01 + matrix[0, 2] * c02
    rows = [[c00, c01, c02], [c01, c11, c12], [c02, c12, c22]]
    return jnp.stack([jnp.stack([entry / determinant for entry in line]) for line in rows])


def cholesky_six(matrix):
    lower = {}
    for first in range(6):
        for second in range(first + 1):
            total = matrix[first, second]
            for inner in range(second):
                total = total - lower[first, inner] * lower[second, inner]
            if first == second:
                lower[first, first] = jnp.sqrt(total)
            else:
                lower[first, second] = total / lower[second, second]
    return lower


def solve_six(lower, target):
    middle = []
    for first in range(6):
        total = target[first]
        for inner in range(first):
            total = total - lower[first, inner] * middle[inner]
        middle.append(total / lower[first, first])
    result = [None] * 6
    for first in reversed(range(6)):
        total = middle[first]
        for inner in range(first + 1, 6):
            total = total - lower[inner, first] * result[inner]
        result[first] = total / lower[first, first]
    return jnp.stack(result)


def point_geometry(jac_cam, jac_pt, resid, damp_value):
    camera_part = jac_cam.reshape((2, 6) + jac_cam.shape[1:])
    point_part = jac_pt.reshape((2, 3) + jac_pt.shape[1:])
    coupling = jnp.sum(camera_part[:, :, None] * point_part[:, None, :], axis=0)
    normal = jnp.sum(point_part[:, :, None] * point_part[:, None, :], axis=(0, 3))
    normal = normal + damp_value * jnp.eye(3, dtype=jac_pt.dtype)[:, :, None]
    point_inverse = invert_three(normal)
    point_rhs = -jnp.sum(point_part * resid[:, None], axis=(0, 2))
    return (camera_part, coupling, point_inverse, point_rhs)


def camera_terms(camera_part, coupling, point_inverse, point_rhs, resid):
    weighted = jnp.sum(coupling[:, :, None] * point_inverse[None, :, :, None, :], axis=1)
    schur_part = jnp.sum(weighted[:, None] * coupling[None], axis=2)
    camera_block = jnp.sum(camera_part[:, :, None] * camera_part[:, None, :], axis=0)
    camera_rhs = -jnp.sum(camera_part * resid[:, None], axis=0) - jnp.sum(
        weighted * point_rhs[None, :, None, :], axis=1
    )
    return jnp.concatenate([pack_sym(camera_block), pack_sym(schur_part), camera_rhs], axis=0)


def point_side(coupling, obs_steps):
    return jnp.sum(coupling * obs_steps[:, None], axis=(0, 2))


def camera_side(coupling, point_inverse, point_sum):
    solved = jnp.sum(point_inverse * point_sum[None], axis=1)
    return jnp.sum(coupling * solved[None, :, None, :], axis=1)


def owner_setup(totals, damp_value):
    upper_block = unpack_sym(totals[:21]) + damp_value * jnp.eye(6, dtype=totals.dtype)[:, :, None]
    diagonal_block = upper_block - unpack_sym(totals[21:42])
    return (upper_block, cholesky_six(diagonal_block), totals[42:48])


def exchange(values):
    features, groups, places, lanes = values.shape
    inner = lanes // OUTER
    t = values.reshape(features, groups, places, OUTER, inner).transpose(4, 1, 3, 2, 0)
    t = t.reshape(inner * groups, OUTER, places, features)
    t = lax.all_to_all(t, INNER_AXES, 0, 0, tiled=True)
    t = lax.all_to_all(t, "z", 1, 1, tiled=True)
    t = t.reshape(inner, groups, OUTER, places, features).transpose(4, 1, 3, 2, 0)
    return t.reshape(features, groups, places, lanes)


def shards(jac_cam, jac_pt, resid, obs_slot, requests, coloring, damping):
    damp_value = damping[0]
    table = requests[0]
    cam_count = coloring.shape[0]
    slot_count = table.size
    flat_slots = obs_slot.reshape(-1)
    camera_part, coupling, point_inverse, point_rhs = point_geometry(
        jac_cam, jac_pt, resid, damp_value
    )
    terms = camera_terms(camera_part, coupling, point_inverse, point_rhs, resid)

    exact = lax.Precision.HIGHEST
    obs_shape = obs_slot.shape

    def slot_picks(part):
        high = flat_slots // part
        low = flat_slots % part
        rows = slot_count // part
        pick_low = (low[None, :] == jnp.arange(part, dtype=jnp.int32)[:, None]).astype(jnp.float32)
        pick_high = high[None, :] == jnp.arange(rows, dtype=jnp.int32)[:, None]
        return rows, pick_low, pick_high

    narrow = slot_picks(128)
    wide = slot_picks(512)

    def slot_totals(values, picks):
        rows, pick_low, pick_high = picks
        features = values.shape[0]
        spread = jnp.where(pick_high[None], values.reshape(features, 1, -1), 0.0)
        summed = jnp.dot(spread.reshape(features * rows, -1), pick_low.T, precision=exact)
        return summed.reshape((features,) + table.shape)

    def at_observations(slot_values):
        rows, pick_low, pick_high = narrow
        features = slot_values.shape[0]
        split = jnp.dot(slot_values.reshape(features * rows, -1), pick_low, precision=exact)
        chosen = jnp.where(pick_high[None], split.reshape(features, rows, -1), 0.0).sum(axis=1)
        return chosen.reshape((features,) + obs_shape)

    sent = jnp.concatenate([slot_totals(terms, wide), table[None].astype(terms.dtype)], axis=0)
    arrived_all = exchange(sent)
    blocks_back = arrived_all[:-1]
    served = arrived_all[-1].astype(jnp.int32).reshape(-1)
    owner_pick = (served[:, None] == jnp.arange(cam_count, dtype=jnp.int32)[None, :]).astype(jnp.float32)

    def owner_sum(received):
        features = received.shape[0]
        return jnp.dot(received.reshape(features, -1), owner_pick, precision=exact)

    totals = owner_sum(blocks_back)

    def share_steps(step_values):
        reply = jnp.dot(step_values, owner_pick.T, precision=exact)
        arrived = exchange(reply.reshape((step_values.shape[0],) + table.shape))
        return at_observations(arrived)

    upper_block, factor, camera_rhs = owner_setup(totals, damp_value)
    colors = [coloring == 0, coloring == 1]
    steps = jnp.where(colors[0][None], solve_six(factor, camera_rhs), 0.0)
    for sweep in range(2 * ROUNDS - 1):
        current = colors[(sweep + 1) % 2]
        point_sum = point_side(coupling, share_steps(steps))
        pushed = camera_side(coupling, point_inverse, point_sum)
        back = exchange(slot_totals(pushed, narrow))
        product = jnp.sum(upper_block * steps[None], axis=1) - owner_sum(back)
        steps = steps + jnp.where(current[None], solve_six(factor, camera_rhs - product), 0.0)
    point_sum = point_side(coupling, share_steps(steps))
    point_step = jnp.sum(point_inverse * (point_rhs - point_sum)[None], axis=1)
    return (steps, point_step)


OUTER = 16
INNER_AXES = ("x", "c", "y")


def solution(mesh):
    npts, ngrp = mesh.shape["pts"], mesh.shape["grp"]
    split = Mesh(mesh.devices.reshape(OUTER, npts // OUTER, 1, ngrp), ("z", "x", "c", "y"))
    every = ("z", "x", "c", "y")
    return jax.shard_map(
        shards,
        mesh=split,
        in_specs=(
            P(None, None, every),
            P(None, None, every),
            P(None, None, every),
            P(None, every),
            P("y", None, None, ("z", "x", "c")),
            P(every),
            P(),
        ),
        out_specs=(P(None, every), P(None, every)),
        check_vma=False,
    )
```

```python
import jax
import jax.numpy as jnp
from jax import lax
from jax.sharding import Mesh, PartitionSpec as P

ROUNDS = 2


UPPER = [(first, second) for first in range(6) for second in range(first, 6)]


def pack_sym(matrix):
    return jnp.stack([matrix[first, second] for first, second in UPPER])


def unpack_sym(packed):
    rows = []
    for first in range(6):
        rows.append(
            jnp.stack(
                [
                    packed[UPPER.index((min(first, second), max(first, second)))]
                    for second in range(6)
                ]
            )
        )
    return jnp.stack(rows)


def invert_three(matrix):
    c00 = matrix[1, 1] * matrix[2, 2] - matrix[1, 2] * matrix[2, 1]
    c01 = matrix[1, 2] * matrix[2, 0] - matrix[1, 0] * matrix[2, 2]
    c02 = matrix[1, 0] * matrix[2, 1] - matrix[1, 1] * matrix[2, 0]
    c11 = matrix[0, 0] * matrix[2, 2] - matrix[0, 2] * matrix[2, 0]
    c12 = matrix[0, 2] * matrix[1, 0] - matrix[0, 0] * matrix[1, 2]
    c22 = matrix[0, 0] * matrix[1, 1] - matrix[0, 1] * matrix[1, 0]
    determinant = matrix[0, 0] * c00 + matrix[0, 1] * c01 + matrix[0, 2] * c02
    rows = [[c00, c01, c02], [c01, c11, c12], [c02, c12, c22]]
    return jnp.stack([jnp.stack([entry / determinant for entry in line]) for line in rows])


def cholesky_six(matrix):
    lower = {}
    for first in range(6):
        for second in range(first + 1):
            total = matrix[first, second]
            for inner in range(second):
                total = total - lower[first, inner] * lower[second, inner]
            if first == second:
                lower[first, first] = jnp.sqrt(total)
            else:
                lower[first, second] = total / lower[second, second]
    return lower


def solve_six(lower, target):
    middle = []
    for first in range(6):
        total = target[first]
        for inner in range(first):
            total = total - lower[first, inner] * middle[inner]
        middle.append(total / lower[first, first])
    result = [None] * 6
    for first in reversed(range(6)):
        total = middle[first]
        for inner in range(first + 1, 6):
            total = total - lower[inner, first] * result[inner]
        result[first] = total / lower[first, first]
    return jnp.stack(result)


def point_geometry(jac_cam, jac_pt, resid, damp_value):
    camera_part = jac_cam.reshape((2, 6) + jac_cam.shape[1:])
    point_part = jac_pt.reshape((2, 3) + jac_pt.shape[1:])
    coupling = jnp.sum(camera_part[:, :, None] * point_part[:, None, :], axis=0)
    normal = jnp.sum(point_part[:, :, None] * point_part[:, None, :], axis=(0, 3))
    normal = normal + damp_value * jnp.eye(3, dtype=jac_pt.dtype)[:, :, None]
    point_inverse = invert_three(normal)
    point_rhs = -jnp.sum(point_part * resid[:, None], axis=(0, 2))
    return (camera_part, coupling, point_inverse, point_rhs)


def camera_terms(camera_part, coupling, point_inverse, point_rhs, resid):
    weighted = jnp.sum(coupling[:, :, None] * point_inverse[None, :, :, None, :], axis=1)
    schur_part = jnp.sum(weighted[:, None] * coupling[None], axis=2)
    camera_block = jnp.sum(camera_part[:, :, None] * camera_part[:, None, :], axis=0)
    camera_rhs = -jnp.sum(camera_part * resid[:, None], axis=0) - jnp.sum(
        weighted * point_rhs[None, :, None, :], axis=1
    )
    return jnp.concatenate([pack_sym(camera_block), pack_sym(schur_part), camera_rhs], axis=0)


def point_side(coupling, obs_steps):
    return jnp.sum(coupling * obs_steps[:, None], axis=(0, 2))


def camera_side(coupling, point_inverse, point_sum):
    solved = jnp.sum(point_inverse * point_sum[None], axis=1)
    return jnp.sum(coupling * solved[None, :, None, :], axis=1)


def owner_setup(totals, damp_value):
    upper_block = unpack_sym(totals[:21]) + damp_value * jnp.eye(6, dtype=totals.dtype)[:, :, None]
    diagonal_block = upper_block - unpack_sym(totals[21:42])
    return (upper_block, cholesky_six(diagonal_block), totals[42:48])


def exchange(values):
    return lax.all_to_all(lax.all_to_all(values, INNER_AXES, 1, 1, tiled=True), "z", 2, 2, tiled=True)


def shards(jac_cam, jac_pt, resid, obs_slot, requests, coloring, damping):
    damp_value = damping[0]
    groups, places, lanes = requests.shape[1:]
    inner = lanes // OUTER
    native = (inner * groups, OUTER, places)
    table = requests[0].reshape(groups, places, OUTER, inner).transpose(3, 0, 2, 1).reshape(native)
    cam_count = coloring.shape[0]
    slot_count = table.size
    plain = obs_slot.reshape(-1)
    owner_grp = plain // (places * lanes)
    place = plain // lanes % places
    owner_pts = plain % lanes
    flat_slots = (
        ((owner_pts % inner) * groups + owner_grp) * OUTER + owner_pts // inner
    ) * places + place
    camera_part, coupling, point_inverse, point_rhs = point_geometry(
        jac_cam, jac_pt, resid, damp_value
    )
    terms = camera_terms(camera_part, coupling, point_inverse, point_rhs, resid)

    exact = lax.Precision.HIGHEST
    obs_shape = obs_slot.shape

    def slot_picks(part):
        high = flat_slots // part
        low = flat_slots % part
        rows = slot_count // part
        pick_low = (low[None, :] == jnp.arange(part, dtype=jnp.int32)[:, None]).astype(jnp.float32)
        pick_high = high[None, :] == jnp.arange(rows, dtype=jnp.int32)[:, None]
        return rows, pick_low, pick_high

    narrow = slot_picks(128)
    wide = slot_picks(512)

    def slot_totals(values, picks):
        rows, pick_low, pick_high = picks
        features = values.shape[0]
        spread = jnp.where(pick_high[None], values.reshape(features, 1, -1), 0.0)
        summed = jnp.dot(spread.reshape(features * rows, -1), pick_low.T, precision=exact)
        return summed.reshape((features,) + native)

    def at_observations(slot_values):
        rows, pick_low, pick_high = narrow
        features = slot_values.shape[0]
        split = jnp.dot(slot_values.reshape(features * rows, -1), pick_low, precision=exact)
        chosen = jnp.where(pick_high[None], split.reshape(features, rows, -1), 0.0).sum(axis=1)
        return chosen.reshape((features,) + obs_shape)

    sent = jnp.concatenate([slot_totals(terms, wide), table[None].astype(terms.dtype)], axis=0)
    arrived_all = exchange(sent)
    blocks_back = arrived_all[:-1]
    served = arrived_all[-1].astype(jnp.int32).reshape(-1)
    owner_pick = (served[:, None] == jnp.arange(cam_count, dtype=jnp.int32)[None, :]).astype(jnp.float32)

    def owner_sum(received):
        features = received.shape[0]
        return jnp.dot(received.reshape(features, -1), owner_pick, precision=exact)

    totals = owner_sum(blocks_back)

    def share_steps(step_values):
        reply = jnp.dot(step_values, owner_pick.T, precision=exact)
        arrived = exchange(reply.reshape((step_values.shape[0],) + native))
        return at_observations(arrived)

    upper_block, factor, camera_rhs = owner_setup(totals, damp_value)
    colors = [coloring == 0, coloring == 1]
    steps = jnp.where(colors[0][None], solve_six(factor, camera_rhs), 0.0)
    for sweep in range(2 * ROUNDS - 1):
        current = colors[(sweep + 1) % 2]
        point_sum = point_side(coupling, share_steps(steps))
        pushed = camera_side(coupling, point_inverse, point_sum)
        back = exchange(slot_totals(pushed, wide))
        product = jnp.sum(upper_block * steps[None], axis=1) - owner_sum(back)
        steps = steps + jnp.where(current[None], solve_six(factor, camera_rhs - product), 0.0)
    point_sum = point_side(coupling, share_steps(steps))
    point_step = jnp.sum(point_inverse * (point_rhs - point_sum)[None], axis=1)
    return (steps, point_step)


OUTER = 16
INNER_AXES = ("x", "c", "y")


def solution(mesh):
    npts, ngrp = mesh.shape["pts"], mesh.shape["grp"]
    split = Mesh(mesh.devices.reshape(OUTER, npts // OUTER, 1, ngrp), ("z", "x", "c", "y"))
    every = ("z", "x", "c", "y")
    return jax.shard_map(
        shards,
        mesh=split,
        in_specs=(
            P(None, None, every),
            P(None, None, every),
            P(None, None, every),
            P(None, every),
            P("y", None, None, ("z", "x", "c")),
            P(every),
            P(),
        ),
        out_specs=(P(None, every), P(None, every)),
        check_vma=False,
    )
```

```python
import jax
import jax.numpy as jnp
from jax import lax
from jax.sharding import Mesh, PartitionSpec as P

ROUNDS = 2


UPPER = [(first, second) for first in range(6) for second in range(first, 6)]


def pack_sym(matrix):
    return jnp.stack([matrix[first, second] for first, second in UPPER])


def unpack_sym(packed):
    rows = []
    for first in range(6):
        rows.append(
            jnp.stack(
                [
                    packed[UPPER.index((min(first, second), max(first, second)))]
                    for second in range(6)
                ]
            )
        )
    return jnp.stack(rows)


def invert_three(matrix):
    c00 = matrix[1, 1] * matrix[2, 2] - matrix[1, 2] * matrix[2, 1]
    c01 = matrix[1, 2] * matrix[2, 0] - matrix[1, 0] * matrix[2, 2]
    c02 = matrix[1, 0] * matrix[2, 1] - matrix[1, 1] * matrix[2, 0]
    c11 = matrix[0, 0] * matrix[2, 2] - matrix[0, 2] * matrix[2, 0]
    c12 = matrix[0, 2] * matrix[1, 0] - matrix[0, 0] * matrix[1, 2]
    c22 = matrix[0, 0] * matrix[1, 1] - matrix[0, 1] * matrix[1, 0]
    determinant = matrix[0, 0] * c00 + matrix[0, 1] * c01 + matrix[0, 2] * c02
    rows = [[c00, c01, c02], [c01, c11, c12], [c02, c12, c22]]
    return jnp.stack([jnp.stack([entry / determinant for entry in line]) for line in rows])


def cholesky_six(matrix):
    lower = {}
    for first in range(6):
        for second in range(first + 1):
            total = matrix[first, second]
            for inner in range(second):
                total = total - lower[first, inner] * lower[second, inner]
            if first == second:
                lower[first, first] = jnp.sqrt(total)
            else:
                lower[first, second] = total / lower[second, second]
    return lower


def solve_six(lower, target):
    middle = []
    for first in range(6):
        total = target[first]
        for inner in range(first):
            total = total - lower[first, inner] * middle[inner]
        middle.append(total / lower[first, first])
    result = [None] * 6
    for first in reversed(range(6)):
        total = middle[first]
        for inner in range(first + 1, 6):
            total = total - lower[inner, first] * result[inner]
        result[first] = total / lower[first, first]
    return jnp.stack(result)


def point_geometry(jac_cam, jac_pt, resid, damp_value):
    camera_part = jac_cam.reshape((2, 6) + jac_cam.shape[1:])
    point_part = jac_pt.reshape((2, 3) + jac_pt.shape[1:])
    coupling = jnp.sum(camera_part[:, :, None] * point_part[:, None, :], axis=0)
    normal = jnp.sum(point_part[:, :, None] * point_part[:, None, :], axis=(0, 3))
    normal = normal + damp_value * jnp.eye(3, dtype=jac_pt.dtype)[:, :, None]
    point_inverse = invert_three(normal)
    point_rhs = -jnp.sum(point_part * resid[:, None], axis=(0, 2))
    return (camera_part, coupling, point_inverse, point_rhs)


def camera_terms(camera_part, coupling, point_inverse, point_rhs, resid):
    weighted = jnp.sum(coupling[:, :, None] * point_inverse[None, :, :, None, :], axis=1)
    schur_part = jnp.sum(weighted[:, None] * coupling[None], axis=2)
    camera_block = jnp.sum(camera_part[:, :, None] * camera_part[:, None, :], axis=0)
    camera_rhs = -jnp.sum(camera_part * resid[:, None], axis=0) - jnp.sum(
        weighted * point_rhs[None, :, None, :], axis=1
    )
    return jnp.concatenate([pack_sym(camera_block), pack_sym(schur_part), camera_rhs], axis=0)


def point_side(coupling, obs_steps):
    return jnp.sum(coupling * obs_steps[:, None], axis=(0, 2))


def camera_side(coupling, point_inverse, point_sum):
    solved = jnp.sum(point_inverse * point_sum[None], axis=1)
    return jnp.sum(coupling * solved[None, :, None, :], axis=1)


def owner_setup(totals, damp_value):
    upper_block = unpack_sym(totals[:21]) + damp_value * jnp.eye(6, dtype=totals.dtype)[:, :, None]
    diagonal_block = upper_block - unpack_sym(totals[21:42])
    return (upper_block, cholesky_six(diagonal_block), totals[42:48])


def exchange(values):
    shaped = values.reshape((values.shape[0] // OUTER, OUTER) + values.shape[1:])
    moved = lax.all_to_all(lax.all_to_all(shaped, INNER_AXES, 0, 0, tiled=True), "z", 1, 1, tiled=True)
    return moved.reshape(values.shape)


def shards(jac_cam, jac_pt, resid, obs_slot, requests, coloring, damping):
    damp_value = damping[0]
    groups, places, lanes = requests.shape[1:]
    inner = lanes // OUTER
    rows = inner * groups * OUTER
    table = requests[0].reshape(groups, places, OUTER, inner).transpose(3, 0, 2, 1).reshape(rows, places)
    cam_count = coloring.shape[0]
    plain = obs_slot.reshape(-1)
    owner_grp = plain // (places * lanes)
    place = plain // lanes % places
    owner_pts = plain % lanes
    row = ((owner_pts % inner) * groups + owner_grp) * OUTER + owner_pts // inner
    camera_part, coupling, point_inverse, point_rhs = point_geometry(
        jac_cam, jac_pt, resid, damp_value
    )
    terms = camera_terms(camera_part, coupling, point_inverse, point_rhs, resid)

    exact = lax.Precision.HIGHEST
    obs_shape = obs_slot.shape
    pick_row = (row[None, :] == jnp.arange(rows, dtype=jnp.int32)[:, None]).astype(jnp.float32)
    pick_place = place[None, :] == jnp.arange(places, dtype=jnp.int32)[:, None]
    contract_rows = (((0,), (0,)), ((), ()))
    contract_obs = (((1,), (1,)), ((), ()))

    def slot_totals(values):
        features = values.shape[0]
        spread = jnp.where(pick_place[:, None], values.reshape(1, features, -1), 0.0)
        spread = spread.reshape(places * features, -1)
        return lax.dot_general(pick_row, spread, contract_obs, precision=exact)

    def at_observations(slot_values):
        features = slot_values.shape[1] // places
        split = lax.dot_general(slot_values, pick_row, contract_rows, precision=exact)
        split = split.reshape(places, features, -1)
        chosen = jnp.where(pick_place[:, None], split, 0.0).sum(axis=0)
        return chosen.reshape((features,) + obs_shape)

    served = exchange(table)
    owner_pick = served[:, :, None] == jnp.arange(cam_count, dtype=jnp.int32)[None, None, :]
    owner_pick = owner_pick.astype(jnp.float32).reshape(rows, places * cam_count)
    diagonal = jnp.eye(places, dtype=jnp.float32)

    def owner_sum(received):
        features = received.shape[1] // places
        both = lax.dot_general(received, owner_pick, contract_rows, precision=exact)
        both = both.reshape(places, features, places, cam_count)
        return jnp.sum(both * diagonal[:, None, :, None], axis=(0, 2))

    totals = owner_sum(exchange(slot_totals(terms)))

    def share_steps(step_values):
        features = step_values.shape[0]
        blocks = diagonal[:, None, :, None] * step_values.T[None, :, None, :]
        blocks = blocks.reshape(places * cam_count, places * features)
        reply = jnp.dot(owner_pick, blocks, precision=exact)
        return at_observations(exchange(reply))

    upper_block, factor, camera_rhs = owner_setup(totals, damp_value)
    colors = [coloring == 0, coloring == 1]
    steps = jnp.where(colors[0][None], solve_six(factor, camera_rhs), 0.0)
    for sweep in range(2 * ROUNDS - 1):
        current = colors[(sweep + 1) % 2]
        point_sum = point_side(coupling, share_steps(steps))
        pushed = camera_side(coupling, point_inverse, point_sum)
        back = exchange(slot_totals(pushed))
        product = jnp.sum(upper_block * steps[None], axis=1) - owner_sum(back)
        steps = steps + jnp.where(current[None], solve_six(factor, camera_rhs - product), 0.0)
    point_sum = point_side(coupling, share_steps(steps))
    point_step = jnp.sum(point_inverse * (point_rhs - point_sum)[None], axis=1)
    return (steps, point_step)


OUTER = 16
INNER_AXES = ("x", "c", "y")


def solution(mesh):
    npts, ngrp = mesh.shape["pts"], mesh.shape["grp"]
    split = Mesh(mesh.devices.reshape(OUTER, npts // OUTER, 1, ngrp), ("z", "x", "c", "y"))
    every = ("z", "x", "c", "y")
    return jax.shard_map(
        shards,
        mesh=split,
        in_specs=(
            P(None, None, every),
            P(None, None, every),
            P(None, None, every),
            P(None, every),
            P("y", None, None, ("z", "x", "c")),
            P(every),
            P(),
        ),
        out_specs=(P(None, every), P(None, every)),
        check_vma=False,
    )
```

```python
import jax
import jax.numpy as jnp
from jax import lax
from jax.sharding import Mesh, PartitionSpec as P

ROUNDS = 2


UPPER = [(first, second) for first in range(6) for second in range(first, 6)]


def pack_sym(matrix):
    return jnp.stack([matrix[first, second] for first, second in UPPER])


def unpack_sym(packed):
    rows = []
    for first in range(6):
        rows.append(
            jnp.stack(
                [
                    packed[UPPER.index((min(first, second), max(first, second)))]
                    for second in range(6)
                ]
            )
        )
    return jnp.stack(rows)


def invert_three(matrix):
    c00 = matrix[1, 1] * matrix[2, 2] - matrix[1, 2] * matrix[2, 1]
    c01 = matrix[1, 2] * matrix[2, 0] - matrix[1, 0] * matrix[2, 2]
    c02 = matrix[1, 0] * matrix[2, 1] - matrix[1, 1] * matrix[2, 0]
    c11 = matrix[0, 0] * matrix[2, 2] - matrix[0, 2] * matrix[2, 0]
    c12 = matrix[0, 2] * matrix[1, 0] - matrix[0, 0] * matrix[1, 2]
    c22 = matrix[0, 0] * matrix[1, 1] - matrix[0, 1] * matrix[1, 0]
    determinant = matrix[0, 0] * c00 + matrix[0, 1] * c01 + matrix[0, 2] * c02
    rows = [[c00, c01, c02], [c01, c11, c12], [c02, c12, c22]]
    return jnp.stack([jnp.stack([entry / determinant for entry in line]) for line in rows])


def cholesky_six(matrix):
    lower = {}
    for first in range(6):
        for second in range(first + 1):
            total = matrix[first, second]
            for inner in range(second):
                total = total - lower[first, inner] * lower[second, inner]
            if first == second:
                lower[first, first] = jnp.sqrt(total)
            else:
                lower[first, second] = total / lower[second, second]
    return lower


def solve_six(lower, target):
    middle = []
    for first in range(6):
        total = target[first]
        for inner in range(first):
            total = total - lower[first, inner] * middle[inner]
        middle.append(total / lower[first, first])
    result = [None] * 6
    for first in reversed(range(6)):
        total = middle[first]
        for inner in range(first + 1, 6):
            total = total - lower[inner, first] * result[inner]
        result[first] = total / lower[first, first]
    return jnp.stack(result)


def point_geometry(jac_cam, jac_pt, resid, damp_value):
    camera_part = jac_cam.reshape((2, 6) + jac_cam.shape[1:])
    point_part = jac_pt.reshape((2, 3) + jac_pt.shape[1:])
    coupling = jnp.sum(camera_part[:, :, None] * point_part[:, None, :], axis=0)
    normal = jnp.sum(point_part[:, :, None] * point_part[:, None, :], axis=(0, 3))
    normal = normal + damp_value * jnp.eye(3, dtype=jac_pt.dtype)[:, :, None]
    point_inverse = invert_three(normal)
    point_rhs = -jnp.sum(point_part * resid[:, None], axis=(0, 2))
    return (camera_part, coupling, point_inverse, point_rhs)


def camera_terms(camera_part, coupling, point_inverse, point_rhs, resid):
    weighted = jnp.sum(coupling[:, :, None] * point_inverse[None, :, :, None, :], axis=1)
    schur_part = jnp.sum(weighted[:, None] * coupling[None], axis=2)
    camera_block = jnp.sum(camera_part[:, :, None] * camera_part[:, None, :], axis=0)
    camera_rhs = -jnp.sum(camera_part * resid[:, None], axis=0) - jnp.sum(
        weighted * point_rhs[None, :, None, :], axis=1
    )
    return jnp.concatenate([pack_sym(camera_block), pack_sym(schur_part), camera_rhs], axis=0)


def point_side(coupling, obs_steps):
    return jnp.sum(coupling * obs_steps[:, None], axis=(0, 2))


def camera_side(coupling, point_inverse, point_sum):
    solved = jnp.sum(point_inverse * point_sum[None], axis=1)
    return jnp.sum(coupling * solved[None, :, None, :], axis=1)


def owner_setup(totals, damp_value):
    upper_block = unpack_sym(totals[:21]) + damp_value * jnp.eye(6, dtype=totals.dtype)[:, :, None]
    diagonal_block = upper_block - unpack_sym(totals[21:42])
    return (upper_block, cholesky_six(diagonal_block), totals[42:48])


def exchange(values):
    shaped = values.reshape((values.shape[0] // OUTER, OUTER) + values.shape[1:])
    moved = lax.all_to_all(lax.all_to_all(shaped, INNER_AXES, 0, 0, tiled=True), "z", 1, 1, tiled=True)
    return moved.reshape(values.shape)


def shards(jac_cam, jac_pt, resid, obs_slot, requests, coloring, damping):
    damp_value = damping[0]
    groups, places, lanes = requests.shape[1:]
    inner = lanes // OUTER
    rows = inner * groups * OUTER
    table = requests[0].reshape(groups, places, OUTER, inner).transpose(3, 0, 2, 1).reshape(rows, places)
    cam_count = coloring.shape[0]
    plain = obs_slot.reshape(-1)
    owner_grp = plain // (places * lanes)
    place = plain // lanes % places
    owner_pts = plain % lanes
    row = ((owner_pts % inner) * groups + owner_grp) * OUTER + owner_pts // inner
    camera_part, coupling, point_inverse, point_rhs = point_geometry(
        jac_cam, jac_pt, resid, damp_value
    )
    terms = camera_terms(camera_part, coupling, point_inverse, point_rhs, resid)

    exact = lax.Precision.HIGHEST
    obs_shape = obs_slot.shape
    pick_row = (row[None, :] == jnp.arange(rows, dtype=jnp.int32)[:, None]).astype(jnp.bfloat16)
    pick_place = place[None, :] == jnp.arange(places, dtype=jnp.int32)[:, None]
    contract_rows = (((0,), (0,)), ((), ()))
    contract_obs = (((1,), (1,)), ((), ()))

    def pieces(values, axis):
        first = values.astype(jnp.bfloat16)
        rest = values - first.astype(jnp.float32)
        second = rest.astype(jnp.bfloat16)
        third = (rest - second.astype(jnp.float32)).astype(jnp.bfloat16)
        return jnp.concatenate([first, second, third], axis=axis)

    def joined(result, axis):
        width = result.shape[axis] // 3
        parts = [lax.slice_in_dim(result, k * width, (k + 1) * width, axis=axis) for k in range(3)]
        return (parts[0] + parts[1]) + parts[2]

    def one_hot_dot(lhs, rhs, dims):
        return lax.dot_general(lhs, rhs, dims, preferred_element_type=jnp.float32)

    def slot_totals(values):
        features = values.shape[0]
        spread = jnp.where(pick_place[:, None], values.reshape(1, features, -1), 0.0)
        spread = pieces(spread.reshape(places * features, -1), 0)
        return joined(one_hot_dot(pick_row, spread, contract_obs), 1)

    def at_observations(slot_values):
        features = slot_values.shape[1] // places
        split = joined(one_hot_dot(pieces(slot_values, 1), pick_row, contract_rows), 0)
        split = split.reshape(places, features, -1)
        chosen = jnp.where(pick_place[:, None], split, 0.0).sum(axis=0)
        return chosen.reshape((features,) + obs_shape)

    served = exchange(table)
    owner_pick = served[:, :, None] == jnp.arange(cam_count, dtype=jnp.int32)[None, None, :]
    owner_pick = owner_pick.astype(jnp.bfloat16).reshape(rows, places * cam_count)
    diagonal = jnp.eye(places, dtype=jnp.float32)

    def owner_sum(received):
        features = received.shape[1] // places
        both = joined(one_hot_dot(pieces(received, 1), owner_pick, contract_rows), 0)
        both = both.reshape(places, features, places, cam_count)
        return jnp.sum(both * diagonal[:, None, :, None], axis=(0, 2))

    totals = owner_sum(exchange(slot_totals(terms)))

    def share_steps(step_values):
        features = step_values.shape[0]
        blocks = diagonal[:, None, :, None] * step_values.T[None, :, None, :]
        blocks = pieces(blocks.reshape(places * cam_count, places * features), 1)
        reply = joined(one_hot_dot(owner_pick, blocks, (((1,), (0,)), ((), ()))), 1)
        return at_observations(exchange(reply))

    upper_block, factor, camera_rhs = owner_setup(totals, damp_value)
    colors = [coloring == 0, coloring == 1]
    steps = jnp.where(colors[0][None], solve_six(factor, camera_rhs), 0.0)
    for sweep in range(2 * ROUNDS - 1):
        current = colors[(sweep + 1) % 2]
        point_sum = point_side(coupling, share_steps(steps))
        pushed = camera_side(coupling, point_inverse, point_sum)
        back = exchange(slot_totals(pushed))
        product = jnp.sum(upper_block * steps[None], axis=1) - owner_sum(back)
        steps = steps + jnp.where(current[None], solve_six(factor, camera_rhs - product), 0.0)
    point_sum = point_side(coupling, share_steps(steps))
    point_step = jnp.sum(point_inverse * (point_rhs - point_sum)[None], axis=1)
    return (steps, point_step)


OUTER = 16
INNER_AXES = ("x", "c", "y")


def solution(mesh):
    npts, ngrp = mesh.shape["pts"], mesh.shape["grp"]
    split = Mesh(mesh.devices.reshape(OUTER, npts // OUTER, 1, ngrp), ("z", "x", "c", "y"))
    every = ("z", "x", "c", "y")
    return jax.shard_map(
        shards,
        mesh=split,
        in_specs=(
            P(None, None, every),
            P(None, None, every),
            P(None, None, every),
            P(None, every),
            P("y", None, None, ("z", "x", "c")),
            P(every),
            P(),
        ),
        out_specs=(P(None, every), P(None, every)),
        check_vma=False,
    )
```

```python
import jax
import jax.numpy as jnp
from jax import lax
from jax.sharding import Mesh, PartitionSpec as P

ROUNDS = 2


UPPER = [(first, second) for first in range(6) for second in range(first, 6)]


def pack_sym(matrix):
    return jnp.stack([matrix[first, second] for first, second in UPPER])


def unpack_sym(packed):
    rows = []
    for first in range(6):
        rows.append(
            jnp.stack(
                [
                    packed[UPPER.index((min(first, second), max(first, second)))]
                    for second in range(6)
                ]
            )
        )
    return jnp.stack(rows)


def invert_three(matrix):
    c00 = matrix[1, 1] * matrix[2, 2] - matrix[1, 2] * matrix[2, 1]
    c01 = matrix[1, 2] * matrix[2, 0] - matrix[1, 0] * matrix[2, 2]
    c02 = matrix[1, 0] * matrix[2, 1] - matrix[1, 1] * matrix[2, 0]
    c11 = matrix[0, 0] * matrix[2, 2] - matrix[0, 2] * matrix[2, 0]
    c12 = matrix[0, 2] * matrix[1, 0] - matrix[0, 0] * matrix[1, 2]
    c22 = matrix[0, 0] * matrix[1, 1] - matrix[0, 1] * matrix[1, 0]
    determinant = matrix[0, 0] * c00 + matrix[0, 1] * c01 + matrix[0, 2] * c02
    rows = [[c00, c01, c02], [c01, c11, c12], [c02, c12, c22]]
    return jnp.stack([jnp.stack([entry / determinant for entry in line]) for line in rows])


def cholesky_six(matrix):
    lower = {}
    for first in range(6):
        for second in range(first + 1):
            total = matrix[first, second]
            for inner in range(second):
                total = total - lower[first, inner] * lower[second, inner]
            if first == second:
                lower[first, first] = jnp.sqrt(total)
            else:
                lower[first, second] = total / lower[second, second]
    return lower


def solve_six(lower, target):
    middle = []
    for first in range(6):
        total = target[first]
        for inner in range(first):
            total = total - lower[first, inner] * middle[inner]
        middle.append(total / lower[first, first])
    result = [None] * 6
    for first in reversed(range(6)):
        total = middle[first]
        for inner in range(first + 1, 6):
            total = total - lower[inner, first] * result[inner]
        result[first] = total / lower[first, first]
    return jnp.stack(result)


def point_geometry(jac_cam, jac_pt, resid, damp_value):
    camera_part = jac_cam.reshape((2, 6) + jac_cam.shape[1:])
    point_part = jac_pt.reshape((2, 3) + jac_pt.shape[1:])
    coupling = jnp.sum(camera_part[:, :, None] * point_part[:, None, :], axis=0)
    normal = jnp.sum(point_part[:, :, None] * point_part[:, None, :], axis=(0, 3))
    normal = normal + damp_value * jnp.eye(3, dtype=jac_pt.dtype)[:, :, None]
    point_inverse = invert_three(normal)
    point_rhs = -jnp.sum(point_part * resid[:, None], axis=(0, 2))
    return (camera_part, coupling, point_inverse, point_rhs)


def camera_terms(camera_part, coupling, point_inverse, point_rhs, resid):
    weighted = jnp.sum(coupling[:, :, None] * point_inverse[None, :, :, None, :], axis=1)
    schur_part = jnp.sum(weighted[:, None] * coupling[None], axis=2)
    camera_block = jnp.sum(camera_part[:, :, None] * camera_part[:, None, :], axis=0)
    camera_rhs = -jnp.sum(camera_part * resid[:, None], axis=0) - jnp.sum(
        weighted * point_rhs[None, :, None, :], axis=1
    )
    return jnp.concatenate([pack_sym(camera_block), pack_sym(schur_part), camera_rhs], axis=0)


def point_side(coupling, obs_steps):
    return jnp.sum(coupling * obs_steps[:, None], axis=(0, 2))


def camera_side(coupling, point_inverse, point_sum):
    solved = jnp.sum(point_inverse * point_sum[None], axis=1)
    return jnp.sum(coupling * solved[None, :, None, :], axis=1)


def owner_setup(totals, damp_value):
    upper_block = unpack_sym(totals[:21]) + damp_value * jnp.eye(6, dtype=totals.dtype)[:, :, None]
    diagonal_block = upper_block - unpack_sym(totals[21:42])
    return (upper_block, cholesky_six(diagonal_block), totals[42:48])


def exchange(values):
    shaped = values.reshape((values.shape[0] // OUTER, OUTER) + values.shape[1:])
    moved = lax.all_to_all(lax.all_to_all(shaped, INNER_AXES, 0, 0, tiled=True), "z", 1, 1, tiled=True)
    return moved.reshape(values.shape)


def shards(jac_cam, jac_pt, resid, obs_slot, requests, coloring, damping):
    damp_value = damping[0]
    groups, places, lanes = requests.shape[1:]
    inner = lanes // OUTER
    rows = inner * groups * OUTER
    table = requests[0].reshape(groups, places, OUTER, inner).transpose(3, 0, 2, 1).reshape(rows, places)
    cam_count = coloring.shape[0]
    plain = obs_slot.reshape(-1)
    owner_grp = plain // (places * lanes)
    place = plain // lanes % places
    owner_pts = plain % lanes
    row = ((owner_pts % inner) * groups + owner_grp) * OUTER + owner_pts // inner
    camera_part, coupling, point_inverse, point_rhs = point_geometry(
        jac_cam, jac_pt, resid, damp_value
    )
    terms = camera_terms(camera_part, coupling, point_inverse, point_rhs, resid)

    exact = lax.Precision.HIGHEST
    obs_shape = obs_slot.shape
    pick_row = (row[None, :] == jnp.arange(rows, dtype=jnp.int32)[:, None]).astype(jnp.bfloat16)
    pick_place = place[None, :] == jnp.arange(places, dtype=jnp.int32)[:, None]
    contract_rows = (((0,), (0,)), ((), ()))
    contract_obs = (((1,), (1,)), ((), ()))

    def pieces(values, axis):
        first = values.astype(jnp.bfloat16)
        rest = values - first.astype(jnp.float32)
        second = rest.astype(jnp.bfloat16)
        third = (rest - second.astype(jnp.float32)).astype(jnp.bfloat16)
        return jnp.concatenate([first, second, third], axis=axis)

    def joined(result, axis):
        width = result.shape[axis] // 3
        parts = [lax.slice_in_dim(result, k * width, (k + 1) * width, axis=axis) for k in range(3)]
        return (parts[0] + parts[1]) + parts[2]

    def one_hot_dot(lhs, rhs, dims):
        return lax.dot_general(lhs, rhs, dims, preferred_element_type=jnp.float32)

    def slot_totals(values):
        features = values.shape[0]
        spread = jnp.where(pick_place[:, None], values.reshape(1, features, -1), 0.0)
        spread = pieces(spread.reshape(places * features, -1), 0)
        return joined(one_hot_dot(pick_row, spread, contract_obs), 1)

    def at_observations(slot_values):
        features = slot_values.shape[1] // places
        split = joined(one_hot_dot(pieces(slot_values, 1), pick_row, contract_rows), 0)
        split = split.reshape(places, features, -1)
        chosen = jnp.where(pick_place[:, None], split, 0.0).sum(axis=0)
        return chosen.reshape((features,) + obs_shape)

    arrived = exchange(jnp.concatenate([slot_totals(terms), table.astype(jnp.float32)], axis=1))
    served = arrived[:, -places:].astype(jnp.int32)
    owner_pick = served[:, :, None] == jnp.arange(cam_count, dtype=jnp.int32)[None, None, :]
    owner_pick = owner_pick.astype(jnp.bfloat16).reshape(rows, places * cam_count)
    diagonal = jnp.eye(places, dtype=jnp.float32)

    def owner_sum(received):
        features = received.shape[1] // places
        both = joined(one_hot_dot(pieces(received, 1), owner_pick, contract_rows), 0)
        both = both.reshape(places, features, places, cam_count)
        return jnp.sum(both * diagonal[:, None, :, None], axis=(0, 2))

    totals = owner_sum(arrived[:, :-places])

    def share_steps(step_values):
        features = step_values.shape[0]
        blocks = diagonal[:, None, :, None] * step_values.T[None, :, None, :]
        blocks = pieces(blocks.reshape(places * cam_count, places * features), 1)
        reply = joined(one_hot_dot(owner_pick, blocks, (((1,), (0,)), ((), ()))), 1)
        return at_observations(exchange(reply))

    upper_block, factor, camera_rhs = owner_setup(totals, damp_value)
    colors = [coloring == 0, coloring == 1]
    steps = jnp.where(colors[0][None], solve_six(factor, camera_rhs), 0.0)
    for sweep in range(2 * ROUNDS - 1):
        current = colors[(sweep + 1) % 2]
        point_sum = point_side(coupling, share_steps(steps))
        pushed = camera_side(coupling, point_inverse, point_sum)
        back = exchange(slot_totals(pushed))
        product = jnp.sum(upper_block * steps[None], axis=1) - owner_sum(back)
        steps = steps + jnp.where(current[None], solve_six(factor, camera_rhs - product), 0.0)
    point_sum = point_side(coupling, share_steps(steps))
    point_step = jnp.sum(point_inverse * (point_rhs - point_sum)[None], axis=1)
    return (steps, point_step)


OUTER = 16
INNER_AXES = ("x", "c", "y")


def solution(mesh):
    npts, ngrp = mesh.shape["pts"], mesh.shape["grp"]
    split = Mesh(mesh.devices.reshape(OUTER, npts // OUTER, 1, ngrp), ("z", "x", "c", "y"))
    every = ("z", "x", "c", "y")
    return jax.shard_map(
        shards,
        mesh=split,
        in_specs=(
            P(None, None, every),
            P(None, None, every),
            P(None, None, every),
            P(None, every),
            P("y", None, None, ("z", "x", "c")),
            P(every),
            P(),
        ),
        out_specs=(P(None, every), P(None, every)),
        check_vma=False,
    )
```

```python
import jax
import jax.numpy as jnp
from jax import lax
from jax.sharding import Mesh, PartitionSpec as P

ROUNDS = 2


UPPER = [(first, second) for first in range(6) for second in range(first, 6)]


def pack_sym(matrix):
    return jnp.stack([matrix[first, second] for first, second in UPPER])


def unpack_sym(packed):
    rows = []
    for first in range(6):
        rows.append(
            jnp.stack(
                [
                    packed[UPPER.index((min(first, second), max(first, second)))]
                    for second in range(6)
                ]
            )
        )
    return jnp.stack(rows)


def invert_three(matrix):
    c00 = matrix[1, 1] * matrix[2, 2] - matrix[1, 2] * matrix[2, 1]
    c01 = matrix[1, 2] * matrix[2, 0] - matrix[1, 0] * matrix[2, 2]
    c02 = matrix[1, 0] * matrix[2, 1] - matrix[1, 1] * matrix[2, 0]
    c11 = matrix[0, 0] * matrix[2, 2] - matrix[0, 2] * matrix[2, 0]
    c12 = matrix[0, 2] * matrix[1, 0] - matrix[0, 0] * matrix[1, 2]
    c22 = matrix[0, 0] * matrix[1, 1] - matrix[0, 1] * matrix[1, 0]
    determinant = matrix[0, 0] * c00 + matrix[0, 1] * c01 + matrix[0, 2] * c02
    rows = [[c00, c01, c02], [c01, c11, c12], [c02, c12, c22]]
    return jnp.stack([jnp.stack([entry / determinant for entry in line]) for line in rows])


def cholesky_six(matrix):
    lower = {}
    for first in range(6):
        for second in range(first + 1):
            total = matrix[first, second]
            for inner in range(second):
                total = total - lower[first, inner] * lower[second, inner]
            if first == second:
                lower[first, first] = jnp.sqrt(total)
            else:
                lower[first, second] = total / lower[second, second]
    return lower


def solve_six(lower, target):
    middle = []
    for first in range(6):
        total = target[first]
        for inner in range(first):
            total = total - lower[first, inner] * middle[inner]
        middle.append(total / lower[first, first])
    result = [None] * 6
    for first in reversed(range(6)):
        total = middle[first]
        for inner in range(first + 1, 6):
            total = total - lower[inner, first] * result[inner]
        result[first] = total / lower[first, first]
    return jnp.stack(result)


def point_geometry(jac_cam, jac_pt, resid, damp_value):
    camera_part = jac_cam.reshape((2, 6) + jac_cam.shape[1:])
    point_part = jac_pt.reshape((2, 3) + jac_pt.shape[1:])
    coupling = jnp.sum(camera_part[:, :, None] * point_part[:, None, :], axis=0)
    normal = jnp.sum(point_part[:, :, None] * point_part[:, None, :], axis=(0, 3))
    normal = normal + damp_value * jnp.eye(3, dtype=jac_pt.dtype)[:, :, None]
    point_inverse = invert_three(normal)
    point_rhs = -jnp.sum(point_part * resid[:, None], axis=(0, 2))
    return (camera_part, coupling, point_inverse, point_rhs)


def camera_terms(camera_part, coupling, point_inverse, point_rhs, resid):
    weighted = jnp.sum(coupling[:, :, None] * point_inverse[None, :, :, None, :], axis=1)
    schur_part = jnp.sum(weighted[:, None] * coupling[None], axis=2)
    camera_block = jnp.sum(camera_part[:, :, None] * camera_part[:, None, :], axis=0)
    camera_rhs = -jnp.sum(camera_part * resid[:, None], axis=0) - jnp.sum(
        weighted * point_rhs[None, :, None, :], axis=1
    )
    return jnp.concatenate([pack_sym(camera_block), pack_sym(schur_part), camera_rhs], axis=0)


def point_side(coupling, obs_steps):
    return jnp.sum(coupling * obs_steps[:, None], axis=(0, 2))


def camera_side(coupling, point_inverse, point_sum):
    solved = jnp.sum(point_inverse * point_sum[None], axis=1)
    return jnp.sum(coupling * solved[None, :, None, :], axis=1)


def owner_setup(totals, damp_value):
    diagonal_block = unpack_sym(totals[:21]) + damp_value * jnp.eye(6, dtype=totals.dtype)[:, :, None]
    return (diagonal_block, cholesky_six(diagonal_block), totals[21:27])


def others_side(coupling, point_inverse, obs_steps):
    own = jnp.sum(coupling * obs_steps[:, None], axis=0)
    rest = jnp.sum(own, axis=1)[:, None] - own
    solved = jnp.sum(point_inverse[:, :, None] * rest[None], axis=1)
    return jnp.sum(coupling * solved[None], axis=1)


def exchange(values):
    shaped = values.reshape((values.shape[0] // OUTER, OUTER) + values.shape[1:])
    moved = lax.all_to_all(lax.all_to_all(shaped, INNER_AXES, 0, 0, tiled=True), "z", 1, 1, tiled=True)
    return moved.reshape(values.shape)


def shards(jac_cam, jac_pt, resid, obs_slot, requests, coloring, damping):
    damp_value = damping[0]
    groups, places, lanes = requests.shape[1:]
    inner = lanes // OUTER
    rows = inner * groups * OUTER
    table = requests[0].reshape(groups, places, OUTER, inner).transpose(3, 0, 2, 1).reshape(rows, places)
    cam_count = coloring.shape[0]
    plain = obs_slot.reshape(-1)
    owner_grp = plain // (places * lanes)
    place = plain // lanes % places
    owner_pts = plain % lanes
    row = ((owner_pts % inner) * groups + owner_grp) * OUTER + owner_pts // inner
    camera_part, coupling, point_inverse, point_rhs = point_geometry(
        jac_cam, jac_pt, resid, damp_value
    )
    full = camera_terms(camera_part, coupling, point_inverse, point_rhs, resid)
    terms = jnp.concatenate([full[:21] - full[21:42], full[42:48]], axis=0)

    exact = lax.Precision.HIGHEST
    obs_shape = obs_slot.shape
    pick_row = (row[None, :] == jnp.arange(rows, dtype=jnp.int32)[:, None]).astype(jnp.bfloat16)
    pick_place = place[None, :] == jnp.arange(places, dtype=jnp.int32)[:, None]
    contract_rows = (((0,), (0,)), ((), ()))
    contract_obs = (((1,), (1,)), ((), ()))

    def pieces(values, axis):
        first = values.astype(jnp.bfloat16)
        rest = values - first.astype(jnp.float32)
        second = rest.astype(jnp.bfloat16)
        third = (rest - second.astype(jnp.float32)).astype(jnp.bfloat16)
        return jnp.concatenate([first, second, third], axis=axis)

    def joined(result, axis):
        width = result.shape[axis] // 3
        parts = [lax.slice_in_dim(result, k * width, (k + 1) * width, axis=axis) for k in range(3)]
        return (parts[0] + parts[1]) + parts[2]

    def one_hot_dot(lhs, rhs, dims):
        return lax.dot_general(lhs, rhs, dims, preferred_element_type=jnp.float32)

    def slot_totals(values):
        features = values.shape[0]
        spread = jnp.where(pick_place[:, None], values.reshape(1, features, -1), 0.0)
        spread = pieces(spread.reshape(places * features, -1), 0)
        return joined(one_hot_dot(pick_row, spread, contract_obs), 1)

    def at_observations(slot_values):
        features = slot_values.shape[1] // places
        split = joined(one_hot_dot(pieces(slot_values, 1), pick_row, contract_rows), 0)
        split = split.reshape(places, features, -1)
        chosen = jnp.where(pick_place[:, None], split, 0.0).sum(axis=0)
        return chosen.reshape((features,) + obs_shape)

    arrived = exchange(jnp.concatenate([slot_totals(terms), table.astype(jnp.float32)], axis=1))
    served = arrived[:, -places:].astype(jnp.int32)
    owner_pick = served[:, :, None] == jnp.arange(cam_count, dtype=jnp.int32)[None, None, :]
    owner_pick = owner_pick.astype(jnp.bfloat16).reshape(rows, places * cam_count)
    diagonal = jnp.eye(places, dtype=jnp.float32)

    def owner_sum(received):
        features = received.shape[1] // places
        both = joined(one_hot_dot(pieces(received, 1), owner_pick, contract_rows), 0)
        both = both.reshape(places, features, places, cam_count)
        return jnp.sum(both * diagonal[:, None, :, None], axis=(0, 2))

    totals = owner_sum(arrived[:, :-places])

    def share_steps(step_values):
        features = step_values.shape[0]
        blocks = diagonal[:, None, :, None] * step_values.T[None, :, None, :]
        blocks = pieces(blocks.reshape(places * cam_count, places * features), 1)
        reply = joined(one_hot_dot(owner_pick, blocks, (((1,), (0,)), ((), ()))), 1)
        return at_observations(exchange(reply))

    diagonal_block, factor, camera_rhs = owner_setup(totals, damp_value)
    colors = [coloring == 0, coloring == 1]
    steps = jnp.where(colors[0][None], solve_six(factor, camera_rhs), 0.0)
    for sweep in range(2 * ROUNDS - 1):
        current = colors[(sweep + 1) % 2]
        pushed = others_side(coupling, point_inverse, share_steps(steps))
        back = exchange(slot_totals(pushed))
        product = jnp.sum(diagonal_block * steps[None], axis=1) - owner_sum(back)
        steps = steps + jnp.where(current[None], solve_six(factor, camera_rhs - product), 0.0)
    point_sum = point_side(coupling, share_steps(steps))
    point_step = jnp.sum(point_inverse * (point_rhs - point_sum)[None], axis=1)
    return (steps, point_step)


OUTER = 16
INNER_AXES = ("x", "c", "y")


def solution(mesh):
    npts, ngrp = mesh.shape["pts"], mesh.shape["grp"]
    split = Mesh(mesh.devices.reshape(OUTER, npts // OUTER, 1, ngrp), ("z", "x", "c", "y"))
    every = ("z", "x", "c", "y")
    return jax.shard_map(
        shards,
        mesh=split,
        in_specs=(
            P(None, None, every),
            P(None, None, every),
            P(None, None, every),
            P(None, every),
            P("y", None, None, ("z", "x", "c")),
            P(every),
            P(),
        ),
        out_specs=(P(None, every), P(None, every)),
        check_vma=False,
    )
```

```python
import jax
import jax.numpy as jnp
from jax import lax
from jax.sharding import Mesh, PartitionSpec as P

ROUNDS = 2


UPPER = [(first, second) for first in range(6) for second in range(first, 6)]


def pack_sym(matrix):
    return jnp.stack([matrix[first, second] for first, second in UPPER])


def unpack_sym(packed):
    rows = []
    for first in range(6):
        rows.append(
            jnp.stack(
                [
                    packed[UPPER.index((min(first, second), max(first, second)))]
                    for second in range(6)
                ]
            )
        )
    return jnp.stack(rows)


def invert_three(matrix):
    c00 = matrix[1, 1] * matrix[2, 2] - matrix[1, 2] * matrix[2, 1]
    c01 = matrix[1, 2] * matrix[2, 0] - matrix[1, 0] * matrix[2, 2]
    c02 = matrix[1, 0] * matrix[2, 1] - matrix[1, 1] * matrix[2, 0]
    c11 = matrix[0, 0] * matrix[2, 2] - matrix[0, 2] * matrix[2, 0]
    c12 = matrix[0, 2] * matrix[1, 0] - matrix[0, 0] * matrix[1, 2]
    c22 = matrix[0, 0] * matrix[1, 1] - matrix[0, 1] * matrix[1, 0]
    determinant = matrix[0, 0] * c00 + matrix[0, 1] * c01 + matrix[0, 2] * c02
    rows = [[c00, c01, c02], [c01, c11, c12], [c02, c12, c22]]
    return jnp.stack([jnp.stack([entry / determinant for entry in line]) for line in rows])


def cholesky_six(matrix):
    lower = {}
    for first in range(6):
        for second in range(first + 1):
            total = matrix[first, second]
            for inner in range(second):
                total = total - lower[first, inner] * lower[second, inner]
            if first == second:
                lower[first, first] = jnp.sqrt(total)
            else:
                lower[first, second] = total / lower[second, second]
    return lower


def solve_six(lower, target):
    middle = []
    for first in range(6):
        total = target[first]
        for inner in range(first):
            total = total - lower[first, inner] * middle[inner]
        middle.append(total / lower[first, first])
    result = [None] * 6
    for first in reversed(range(6)):
        total = middle[first]
        for inner in range(first + 1, 6):
            total = total - lower[inner, first] * result[inner]
        result[first] = total / lower[first, first]
    return jnp.stack(result)


def point_geometry(jac_cam, jac_pt, resid, damp_value):
    camera_part = jac_cam.reshape((2, 6) + jac_cam.shape[1:])
    point_part = jac_pt.reshape((2, 3) + jac_pt.shape[1:])
    coupling = jnp.sum(camera_part[:, :, None] * point_part[:, None, :], axis=0)
    normal = jnp.sum(point_part[:, :, None] * point_part[:, None, :], axis=(0, 3))
    normal = normal + damp_value * jnp.eye(3, dtype=jac_pt.dtype)[:, :, None]
    point_inverse = invert_three(normal)
    point_rhs = -jnp.sum(point_part * resid[:, None], axis=(0, 2))
    return (camera_part, coupling, point_inverse, point_rhs)


def camera_terms(camera_part, coupling, point_inverse, point_rhs, resid):
    weighted = jnp.sum(coupling[:, :, None] * point_inverse[None, :, :, None, :], axis=1)
    schur_part = jnp.sum(weighted[:, None] * coupling[None], axis=2)
    camera_block = jnp.sum(camera_part[:, :, None] * camera_part[:, None, :], axis=0)
    camera_rhs = -jnp.sum(camera_part * resid[:, None], axis=0) - jnp.sum(
        weighted * point_rhs[None, :, None, :], axis=1
    )
    return jnp.concatenate([pack_sym(camera_block), pack_sym(schur_part), camera_rhs], axis=0)


def point_side(coupling, obs_steps):
    return jnp.sum(coupling * obs_steps[:, None], axis=(0, 2))


def camera_side(coupling, point_inverse, point_sum):
    solved = jnp.sum(point_inverse * point_sum[None], axis=1)
    return jnp.sum(coupling * solved[None, :, None, :], axis=1)


def owner_setup(totals, damp_value):
    diagonal_block = unpack_sym(totals[:21]) + damp_value * jnp.eye(6, dtype=totals.dtype)[:, :, None]
    return (diagonal_block, cholesky_six(diagonal_block), totals[21:27])


def others_side(coupling, point_inverse, obs_steps):
    own = jnp.sum(coupling * obs_steps[:, None], axis=0)
    rest = jnp.sum(own, axis=1)[:, None] - own
    solved = jnp.sum(point_inverse[:, :, None] * rest[None], axis=1)
    return jnp.sum(coupling * solved[None], axis=1)


def exchange(values):
    rows, cols = values.shape
    first = lax.all_to_all(values.reshape(rows // OUTER, OUTER * cols), INNER_AXES, 0, 0, tiled=True)
    turned = first.reshape(rows // OUTER, OUTER, cols).transpose(1, 0, 2).reshape(OUTER, rows // OUTER * cols)
    moved = lax.all_to_all(turned, "z", 0, 0, tiled=True)
    return moved.reshape(OUTER, rows // OUTER, cols).transpose(1, 0, 2).reshape(rows, cols)


def shards(jac_cam, jac_pt, resid, obs_slot, requests, coloring, damping):
    damp_value = damping[0]
    groups, places, lanes = requests.shape[1:]
    inner = lanes // OUTER
    rows = inner * groups * OUTER
    table = requests[0].reshape(groups, places, OUTER, inner).transpose(3, 0, 2, 1).reshape(rows, places)
    cam_count = coloring.shape[0]
    plain = obs_slot.reshape(-1)
    owner_grp = plain // (places * lanes)
    place = plain // lanes % places
    owner_pts = plain % lanes
    row = ((owner_pts % inner) * groups + owner_grp) * OUTER + owner_pts // inner
    camera_part, coupling, point_inverse, point_rhs = point_geometry(
        jac_cam, jac_pt, resid, damp_value
    )
    full = camera_terms(camera_part, coupling, point_inverse, point_rhs, resid)
    terms = jnp.concatenate([full[:21] - full[21:42], full[42:48]], axis=0)

    exact = lax.Precision.HIGHEST
    obs_shape = obs_slot.shape
    pick_row = (row[None, :] == jnp.arange(rows, dtype=jnp.int32)[:, None]).astype(jnp.bfloat16)
    pick_place = place[None, :] == jnp.arange(places, dtype=jnp.int32)[:, None]
    contract_rows = (((0,), (0,)), ((), ()))
    contract_obs = (((1,), (1,)), ((), ()))

    def pieces(values, axis):
        first = values.astype(jnp.bfloat16)
        rest = values - first.astype(jnp.float32)
        second = rest.astype(jnp.bfloat16)
        third = (rest - second.astype(jnp.float32)).astype(jnp.bfloat16)
        return jnp.concatenate([first, second, third], axis=axis)

    def joined(result, axis):
        width = result.shape[axis] // 3
        parts = [lax.slice_in_dim(result, k * width, (k + 1) * width, axis=axis) for k in range(3)]
        return (parts[0] + parts[1]) + parts[2]

    def one_hot_dot(lhs, rhs, dims):
        return lax.dot_general(lhs, rhs, dims, preferred_element_type=jnp.float32)

    def slot_totals(values):
        features = values.shape[0]
        spread = jnp.where(pick_place[:, None], values.reshape(1, features, -1), 0.0)
        spread = pieces(spread.reshape(places * features, -1), 0)
        return joined(one_hot_dot(pick_row, spread, contract_obs), 1)

    def at_observations(slot_values):
        features = slot_values.shape[1] // places
        split = joined(one_hot_dot(pieces(slot_values, 1), pick_row, contract_rows), 0)
        split = split.reshape(places, features, -1)
        chosen = jnp.where(pick_place[:, None], split, 0.0).sum(axis=0)
        return chosen.reshape((features,) + obs_shape)

    arrived = exchange(jnp.concatenate([slot_totals(terms), table.astype(jnp.float32)], axis=1))
    served = arrived[:, -places:].astype(jnp.int32)
    owner_pick = served[:, :, None] == jnp.arange(cam_count, dtype=jnp.int32)[None, None, :]
    owner_pick = owner_pick.astype(jnp.bfloat16).reshape(rows, places * cam_count)
    diagonal = jnp.eye(places, dtype=jnp.float32)

    def owner_sum(received):
        features = received.shape[1] // places
        both = joined(one_hot_dot(pieces(received, 1), owner_pick, contract_rows), 0)
        both = both.reshape(places, features, places, cam_count)
        return jnp.sum(both * diagonal[:, None, :, None], axis=(0, 2))

    totals = owner_sum(arrived[:, :-places])

    def share_steps(step_values):
        features = step_values.shape[0]
        blocks = diagonal[:, None, :, None] * step_values.T[None, :, None, :]
        blocks = pieces(blocks.reshape(places * cam_count, places * features), 1)
        reply = joined(one_hot_dot(owner_pick, blocks, (((1,), (0,)), ((), ()))), 1)
        return at_observations(exchange(reply))

    diagonal_block, factor, camera_rhs = owner_setup(totals, damp_value)
    colors = [coloring == 0, coloring == 1]
    steps = jnp.where(colors[0][None], solve_six(factor, camera_rhs), 0.0)
    for sweep in range(2 * ROUNDS - 1):
        current = colors[(sweep + 1) % 2]
        pushed = others_side(coupling, point_inverse, share_steps(steps))
        back = exchange(slot_totals(pushed))
        product = jnp.sum(diagonal_block * steps[None], axis=1) - owner_sum(back)
        steps = steps + jnp.where(current[None], solve_six(factor, camera_rhs - product), 0.0)
    point_sum = point_side(coupling, share_steps(steps))
    point_step = jnp.sum(point_inverse * (point_rhs - point_sum)[None], axis=1)
    return (steps, point_step)


OUTER = 16
INNER_AXES = ("x", "c", "y")


def solution(mesh):
    npts, ngrp = mesh.shape["pts"], mesh.shape["grp"]
    split = Mesh(mesh.devices.reshape(OUTER, npts // OUTER, 1, ngrp), ("z", "x", "c", "y"))
    every = ("z", "x", "c", "y")
    return jax.shard_map(
        shards,
        mesh=split,
        in_specs=(
            P(None, None, every),
            P(None, None, every),
            P(None, None, every),
            P(None, every),
            P("y", None, None, ("z", "x", "c")),
            P(every),
            P(),
        ),
        out_specs=(P(None, every), P(None, every)),
        check_vma=False,
    )
```
